512 devices in a mesh: tm: 32 (over z, core), tile: 16 (over y, x).
Axes of the slice: x: 4, y: 4, z: 16, core: 2. Of those that a mesh axis runs over, the one named last changes fastest.
Arguments:
- tile_rows: int32 [32, 1024], P('tm', 'tile'), may hold values from 0 to 31
- tile_cols: int32 [32, 1024], P('tm', 'tile'), may hold values from 0 to 7
- live_tiles: int32 [32, 16], P('tm', 'tile'), may hold values from 32 to 64, as said below
- factor_tiles: bfloat16 [32, 1024, 128, 128], P('tm', 'tile'), may hold values from -0.09375 to 0.09375
- bus_inverse: bfloat16 [32, 128, 128, 128], P('tm', 'tile'), may hold values from -0.5 to 0.5
- bus_coupling: bfloat16 [32, 128, 128, 128], P('tm', 'tile'), may hold values from -0.5 to 0.5
- bus_rhs: bfloat16 [32, 128, 64, 128], P('tm', 'tile'), may hold values from -6 to 6
- row_inverse: bfloat16 [32, 32, 128, 128], P('tm', 'tile'), may hold values from -0.5 to 0.5
- row_rhs: bfloat16 [32, 32, 64, 128], P('tm', 'tile'), may hold values from -6 to 6
- coupling_inverse: float32 [32, 128, 128], P('tm')
- coupling_next: float32 [32, 128, 128], P('tm')
- coupling_rhs: float32 [32, 64, 128], P('tm'), may hold values from -6 to 6
Outputs:
- multipliers: float32 [32, 64, 128], P('tm')
- bus_values: bfloat16 [32, 128, 64, 128], P('tm', 'tile')
- row_values: float32 [32, 32, 64, 128], P('tm', 'tile')
The draws below stay inside these ranges and needn't reach their ends.
Inputs may be any that keep to these rules, and one draw needn't show every extreme that they name: `live_tiles`: at least one device uses all 64 of its slots.
All inputs are finite; a program needn't handle non-finite values.
Results may differ from the reference program's by a relative error of at most 0.006.
Values sent between devices are 32-bit elements; how exact they have to be, the bound alone decides.
No kernel may reach another device: no remote copies, remote signals or barrier semaphores. Data moves between devices by JAX's collectives and lax.ppermute only.
A program may use at most 64 MiB of HBM per device.

```python
import math
import jax
import jax.numpy as jnp
from jax import lax

BLOCK = 128
VECTORS = 64
TILES_DEV = 64
BUS_DEV = 8
ROWS_DEV = 2
SECTIONS = 32
GROUP = 16
TILES = 1024
BUSES = 128
BLOCK_ROWS = 32


def draw_live_tiles(key, part):
    first, second = jax.random.split(key)
    counts = jax.random.randint(first, (SECTIONS * GROUP,), TILES_DEV // 2, TILES_DEV + 1)
    chosen = jax.random.randint(second, (), 0, SECTIONS * GROUP)
    counts = jnp.where(jnp.arange(SECTIONS * GROUP) == chosen, TILES_DEV, counts)
    return counts.reshape(SECTIONS, GROUP).astype(jnp.int32)


def dominant_block(key, lowest, highest):
    first, second = jax.random.split(key, 2)
    diagonal = jax.random.uniform(first, (SECTIONS, BLOCK), jnp.float32, lowest, highest)
    bound = 0.26 / math.sqrt(BLOCK)
    noise = jax.random.uniform(second, (SECTIONS, BLOCK, BLOCK), jnp.float32, -bound, bound)
    eye = jnp.eye(BLOCK, dtype=jnp.float32)
    return (noise * (1.0 - eye) + eye * diagonal[:, None, :]).astype(jnp.float32)


def draw_coupling_inverse(key, part):
    return dominant_block(jax.random.fold_in(key, 11), 0.95, 1.0)


def draw_coupling_next(key, part):
    return dominant_block(jax.random.fold_in(key, 23), 0.9, 1.0)


def plant(result, rng, smallest, largest):
    longest = result.shape.index(max(result.shape))
    spots = []
    for shift in (0, 1):
        where = [jax.random.randint(jax.random.fold_in(rng, axis), (), 0, length) for axis, length in enumerate(result.shape)]
        where[longest] = (where[longest] + shift) % result.shape[longest]
        spots.append(tuple(where))
    return result.at[spots[0]].set(smallest).at[spots[1]].set(largest)


def shard_levels(key, shape, pieces, smallest, high):
    def one(axis_at, parts):
        draws = jax.random.uniform(jax.random.fold_in(jax.random.fold_in(key, 6), axis_at), (parts,), jnp.float32, smallest / len(pieces), high / len(pieces))
        return jnp.repeat(jnp.exp(draws), shape[axis_at] // parts).reshape((-1,) + (1,) * (len(shape) - axis_at - 1))

    loudness = one(*pieces[0])
    for cut in pieces[1:]:
        loudness = loudness * one(*cut)
    return loudness


def bell_draw(stream_key, shape, deviation, most, cuts=(), kind=jnp.bfloat16):
    drawn = deviation * jax.random.normal(stream_key, shape, jnp.float32)
    if cuts:
        drawn = drawn * shard_levels(stream_key, shape, cuts, -0.22, 0.18)
    return jnp.clip(drawn, -most, most).astype(kind)


def setup_inputs(seed: int = 0) -> dict:
    key_of = jax.random.split(jax.random.key(seed), 13)
    return {
        "tile_rows": plant(jax.random.randint(key_of[0], (SECTIONS, TILES), 0, BLOCK_ROWS), jax.random.fold_in(key_of[0], 1), 0, BLOCK_ROWS - 1).astype(jnp.int32),
        "tile_cols": plant(jax.random.randint(key_of[1], (SECTIONS, TILES), 0, BUS_DEV), jax.random.fold_in(key_of[1], 1), 0, BUS_DEV - 1).astype(jnp.int32),
        "live_tiles": draw_live_tiles(jax.random.fold_in(key_of[12], 71), 0),
        "factor_tiles": bell_draw(key_of[3], (SECTIONS, TILES, BLOCK, BLOCK), (BLOCK * TILES_DEV // ROWS_DEV) ** -0.5, 0.09375, ((0, 32), (1, 16))),
        "bus_inverse": bell_draw(key_of[4], (SECTIONS, BUSES, BLOCK, BLOCK), BLOCK ** -0.5, 0.5, ((0, 32), (1, 16))),
        "bus_coupling": bell_draw(key_of[5], (SECTIONS, BUSES, BLOCK, BLOCK), BLOCK ** -0.5, 0.5, ((0, 32), (1, 16))),
        "bus_rhs": bell_draw(key_of[6], (SECTIONS, BUSES, VECTORS, BLOCK), 1.0, 6.0, ((0, 32), (1, 16))),
        "row_inverse": bell_draw(key_of[7], (SECTIONS, BLOCK_ROWS, BLOCK, BLOCK), BLOCK ** -0.5, 0.5, ((0, 32), (1, 16))),
        "row_rhs": bell_draw(key_of[8], (SECTIONS, BLOCK_ROWS, VECTORS, BLOCK), 1.0, 6.0, ((0, 32), (1, 16))),
        "coupling_inverse": draw_coupling_inverse(jax.random.fold_in(key_of[12], 71), 0),
        "coupling_next": draw_coupling_next(jax.random.fold_in(key_of[12], 71), 0),
        "coupling_rhs": bell_draw(key_of[11], (SECTIONS, VECTORS, BLOCK), 1.0, 6.0, ((0, 32),), jnp.float32),
    }


HIGH = lax.Precision.HIGHEST


def reference(tile_rows, tile_cols, live_tiles, factor_tiles, bus_inverse, bus_coupling, bus_rhs, row_inverse, row_rhs, coupling_inverse, coupling_next, coupling_rhs):
    def chain(beyond, items):
        inverse, nextmat, rhside = items
        here = jnp.dot(rhside - jnp.dot(beyond, nextmat, precision=HIGH), inverse, precision=HIGH)
        return here, here

    start = jnp.zeros((VECTORS, BLOCK), jnp.float32)
    _, multipliers = lax.scan(chain, start, (coupling_inverse, coupling_next, coupling_rhs), reverse=True)
    rounded = multipliers.astype(jnp.bfloat16)
    coupled = jnp.einsum('srb,sjbc->sjrc', rounded.astype(jnp.float32), bus_coupling.astype(jnp.float32), precision=HIGH)
    bus_work = (bus_rhs.astype(jnp.float32) - coupled).astype(jnp.bfloat16)
    bus_values = jnp.einsum('sjrb,sjbc->sjrc', bus_work.astype(jnp.float32), bus_inverse.astype(jnp.float32), precision=HIGH).astype(jnp.bfloat16)

    owner_group = (jnp.arange(TILES) // TILES_DEV).astype(jnp.int32)
    slot_index = (jnp.arange(TILES) % TILES_DEV).astype(jnp.int32)
    row_range = jnp.arange(BLOCK_ROWS).astype(jnp.int32)

    def section(items):
        rows, cols, live, tiles, buses = items
        global_col = (owner_group * BUS_DEV + cols).astype(jnp.int32)
        chosen = buses[global_col]
        live_mask = (slot_index < live[owner_group]).astype(jnp.float32)
        products = jnp.einsum('krb,kbc->krc', chosen.astype(jnp.float32), tiles.astype(jnp.float32), precision=HIGH)
        products = products * live_mask[:, None, None]
        onehot = (rows[:, None] == row_range[None, :]).astype(jnp.float32)
        return jnp.einsum('ki,krc->irc', onehot, products, precision=HIGH)

    partials = lax.map(section, (tile_rows, tile_cols, live_tiles, factor_tiles, bus_values))
    row_work = (row_rhs.astype(jnp.float32) - partials).astype(jnp.bfloat16)
    row_values = jnp.einsum('sirb,sibc->sirc', row_work.astype(jnp.float32), row_inverse.astype(jnp.float32), precision=HIGH)
    return (multipliers, bus_values, row_values)
```

```python
import jax
import jax.numpy as jnp
from jax import lax
from jax.sharding import PartitionSpec as P

HIGH = lax.Precision.HIGHEST
REDUCE = "alltoall"


def pulled_from(x, axis, by):
    size = lax.axis_size(axis)
    pairs = [(i + by, i) for i in range(size) if i + by < size]
    return lax.ppermute(x, axis, pairs)


def chain_multipliers(inverse, nextmat, rhside):
    vectors = rhside.shape[0]
    b = jnp.dot(rhside, inverse, precision=HIGH)
    a = -jnp.dot(nextmat, inverse, precision=HIGH)
    size = lax.axis_size("tm")
    by = 1
    while by < size:
        if by * 2 < size:
            got = pulled_from(jnp.concatenate([b, a], axis=0), "tm", by)
            got_b, got_a = got[:vectors], got[vectors:]
            b = b + jnp.dot(got_b, a, precision=HIGH)
            a = jnp.dot(got_a, a, precision=HIGH)
        else:
            got_b = pulled_from(b, "tm", by)
            b = b + jnp.dot(got_b, a, precision=HIGH)
        by *= 2
    return b


def per_device(
    tile_rows,
    tile_cols,
    live_tiles,
    factor_tiles,
    bus_inverse,
    bus_coupling,
    bus_rhs,
    row_inverse,
    row_rhs,
    coupling_inverse,
    coupling_next,
    coupling_rhs,
):
    multipliers = chain_multipliers(coupling_inverse[0], coupling_next[0], coupling_rhs[0])
    rounded = multipliers.astype(jnp.bfloat16)
    coupled = jnp.einsum(
        "rb,jbc->jrc", rounded, bus_coupling[0], preferred_element_type=jnp.float32
    )
    bus_work = (bus_rhs[0].astype(jnp.float32) - coupled).astype(jnp.bfloat16)
    bus_values = jnp.einsum(
        "jrb,jbc->jrc", bus_work, bus_inverse[0], preferred_element_type=jnp.float32
    ).astype(jnp.bfloat16)
    rows = tile_rows[0]
    cols = tile_cols[0]
    slots = rows.shape[0]
    buses_here = bus_values.shape[0]
    select_table = (cols[:, None] == jnp.arange(buses_here)[None, :]).astype(jnp.bfloat16)
    chosen = jnp.einsum(
        "kj,jrb->krb", select_table, bus_values, preferred_element_type=jnp.float32
    ).astype(jnp.bfloat16)
    live_mask = (jnp.arange(slots) < live_tiles[0, 0]).astype(jnp.float32)
    products = jnp.einsum(
        "krb,kbc->krc", chosen, factor_tiles[0], preferred_element_type=jnp.float32
    )
    products = products * live_mask[:, None, None]
    owned = row_rhs.shape[1]
    group = lax.axis_size("tile")
    total_rows = owned * group
    onehot = (rows[:, None] == jnp.arange(total_rows)[None, :]).astype(jnp.float32)
    whole = jnp.einsum("ki,krc->irc", onehot, products, precision=HIGH)
    if REDUCE == "scatter":
        partials = lax.psum_scatter(whole, "tile", scatter_dimension=0, tiled=True)
    elif REDUCE == "alltoall":
        spread = lax.all_to_all(whole, "tile", 0, 0, tiled=True)
        partials = spread.reshape((group, owned) + spread.shape[1:]).sum(axis=0)
    else:
        summed = lax.psum(whole, "tile")
        partials = lax.dynamic_slice_in_dim(summed, lax.axis_index("tile") * owned, owned, 0)
    row_work = (row_rhs[0].astype(jnp.float32) - partials).astype(jnp.bfloat16)
    row_values = jnp.einsum(
        "irb,ibc->irc", row_work, row_inverse[0], preferred_element_type=jnp.float32
    )
    return (multipliers[None], bus_values[None], row_values[None])


def solution(mesh):
    placed = (
        P("tm", "tile"),
        P("tm", "tile"),
        P("tm", "tile"),
        P("tm", "tile", None, None),
        P("tm", "tile", None, None),
        P("tm", "tile", None, None),
        P("tm", "tile", None, None),
        P("tm", "tile", None, None),
        P("tm", "tile", None, None),
        P("tm", None, None),
        P("tm", None, None),
        P("tm", None, None),
    )
    return jax.shard_map(
        per_device,
        mesh=mesh,
        in_specs=placed,
        out_specs=(P("tm", None, None), P("tm", "tile", None, None), P("tm", "tile", None, None)),
        check_vma=False,
    )
```

```python
import jax
import jax.numpy as jnp
from jax import lax
from jax.sharding import PartitionSpec as P

HIGH = lax.Precision.HIGHEST


def pulled_from(x, axis, by):
    size = lax.axis_size(axis)
    pairs = [(i + by, i) for i in range(size) if i + by < size]
    return lax.ppermute(x, axis, pairs)


def chain_multipliers(inverse, nextmat, rhside):
    vectors = rhside.shape[0]
    b = jnp.dot(rhside, inverse, precision=HIGH)
    a = -jnp.dot(nextmat, inverse, precision=HIGH)
    size = lax.axis_size("tm")
    by = 1
    while by < size:
        if by * 4 == size:
            b = b + jnp.dot(pulled_from(b, "tm", by), a, precision=HIGH)
            ahead = jnp.dot(pulled_from(b, "tm", by), a, precision=HIGH)
            b = b + jnp.dot(pulled_from(ahead, "tm", by), a, precision=HIGH)
            break
        got = pulled_from(jnp.concatenate([b, a], axis=0), "tm", by)
        got_b, got_a = got[:vectors], got[vectors:]
        b = b + jnp.dot(got_b, a, precision=HIGH)
        if by * 2 < size:
            a = jnp.dot(got_a, a, precision=HIGH)
        by *= 2
    return b


def per_device(
    tile_rows,
    tile_cols,
    live_tiles,
    factor_tiles,
    bus_inverse,
    bus_coupling,
    bus_rhs,
    row_inverse,
    row_rhs,
    coupling_inverse,
    coupling_next,
    coupling_rhs,
):
    multipliers = chain_multipliers(coupling_inverse[0], coupling_next[0], coupling_rhs[0])
    rounded = multipliers.astype(jnp.bfloat16)
    coupled = jnp.einsum(
        "rb,jbc->jrc", rounded, bus_coupling[0], preferred_element_type=jnp.float32
    )
    bus_work = (bus_rhs[0].astype(jnp.float32) - coupled).astype(jnp.bfloat16)
    bus_values = jnp.einsum(
        "jrb,jbc->jrc", bus_work, bus_inverse[0], preferred_element_type=jnp.float32
    ).astype(jnp.bfloat16)
    rows = tile_rows[0]
    cols = tile_cols[0]
    slots = rows.shape[0]
    buses_here = bus_values.shape[0]
    select_table = (cols[:, None] == jnp.arange(buses_here)[None, :]).astype(jnp.bfloat16)
    chosen = jnp.einsum(
        "kj,jrb->krb", select_table, bus_values, preferred_element_type=jnp.float32
    ).astype(jnp.bfloat16)
    live = jnp.arange(slots) < live_tiles[0, 0]
    products = jnp.einsum(
        "krb,kbc->krc", chosen, factor_tiles[0], preferred_element_type=jnp.float32
    )
    owned = row_rhs.shape[1]
    group = lax.axis_size("tile")
    total_rows = owned * group
    placed_in = (jnp.arange(total_rows)[:, None] == rows[None, :]) & live[None, :]
    whole = jnp.dot(
        placed_in.astype(jnp.float32), products.reshape(slots, -1), precision=HIGH
    ).reshape((total_rows,) + products.shape[1:])
    spread = lax.all_to_all(whole, "tile", 0, 0, tiled=True)
    partials = spread.reshape((group, owned) + spread.shape[1:]).sum(axis=0)
    row_work = (row_rhs[0].astype(jnp.float32) - partials).astype(jnp.bfloat16)
    row_values = jnp.einsum(
        "irb,ibc->irc", row_work, row_inverse[0], preferred_element_type=jnp.float32
    )
    return (multipliers[None], bus_values[None], row_values[None])


def solution(mesh):
    placed = (
        P("tm", "tile"),
        P("tm", "tile"),
        P("tm", "tile"),
        P("tm", "tile", None, None),
        P("tm", "tile", None, None),
        P("tm", "tile", None, None),
        P("tm", "tile", None, None),
        P("tm", "tile", None, None),
        P("tm", "tile", None, None),
        P("tm", None, None),
        P("tm", None, None),
        P("tm", None, None),
    )
    return jax.shard_map(
        per_device,
        mesh=mesh,
        in_specs=placed,
        out_specs=(P("tm", None, None), P("tm", "tile", None, None), P("tm", "tile", None, None)),
        check_vma=False,
    )
```

```python
import jax
import jax.numpy as jnp
from jax import lax
from jax.sharding import PartitionSpec as P

HIGH = lax.Precision.HIGHEST


def pulled_from(x, axis, by):
    size = lax.axis_size(axis)
    pairs = [(i + by, i) for i in range(size) if i + by < size]
    return lax.ppermute(x, axis, pairs)


def chain_multipliers(inverse, nextmat, rhside):
    vectors = rhside.shape[0]
    b = jnp.dot(rhside, inverse, precision=HIGH)
    a = -jnp.dot(nextmat, inverse, precision=HIGH)
    size = lax.axis_size("tm")
    by = 1
    if size >= 8:
        held = jnp.concatenate([b, a], axis=0)
        got = [pulled_from(held, "tm", k) for k in (1, 2, 3)]
        carry = got[2]
        for step in (got[1], got[0], held):
            carry = jnp.dot(carry, step[vectors:], precision=HIGH)
            carry = carry.at[:vectors].add(step[:vectors])
        b, a = carry[:vectors], carry[vectors:]
        by = 4
    while by < size:
        if by * 4 == size:
            b = b + jnp.dot(pulled_from(b, "tm", by), a, precision=HIGH)
            ahead = jnp.dot(pulled_from(b, "tm", by), a, precision=HIGH)
            b = b + jnp.dot(pulled_from(ahead, "tm", by), a, precision=HIGH)
            break
        got = pulled_from(jnp.concatenate([b, a], axis=0), "tm", by)
        got_b, got_a = got[:vectors], got[vectors:]
        b = b + jnp.dot(got_b, a, precision=HIGH)
        if by * 2 < size:
            a = jnp.dot(got_a, a, precision=HIGH)
        by *= 2
    return b


def per_device(
    tile_rows,
    tile_cols,
    live_tiles,
    factor_tiles,
    bus_inverse,
    bus_coupling,
    bus_rhs,
    row_inverse,
    row_rhs,
    coupling_inverse,
    coupling_next,
    coupling_rhs,
):
    multipliers = chain_multipliers(coupling_inverse[0], coupling_next[0], coupling_rhs[0])
    rounded = multipliers.astype(jnp.bfloat16)
    coupled = jnp.einsum(
        "rb,jbc->jrc", rounded, bus_coupling[0], preferred_element_type=jnp.float32
    )
    bus_work = (bus_rhs[0].astype(jnp.float32) - coupled).astype(jnp.bfloat16)
    bus_values = jnp.einsum(
        "jrb,jbc->jrc", bus_work, bus_inverse[0], preferred_element_type=jnp.float32
    ).astype(jnp.bfloat16)
    rows = tile_rows[0]
    cols = tile_cols[0]
    slots = rows.shape[0]
    buses_here = bus_values.shape[0]
    select_table = (cols[:, None] == jnp.arange(buses_here)[None, :]).astype(jnp.bfloat16)
    chosen = jnp.einsum(
        "kj,jrb->krb", select_table, bus_values, preferred_element_type=jnp.float32
    ).astype(jnp.bfloat16)
    live = jnp.arange(slots) < live_tiles[0, 0]
    products = jnp.einsum(
        "krb,kbc->krc", chosen, factor_tiles[0], preferred_element_type=jnp.float32
    )
    owned = row_rhs.shape[1]
    group = lax.axis_size("tile")
    total_rows = owned * group
    placed_in = (jnp.arange(total_rows)[:, None] == rows[None, :]) & live[None, :]
    whole = jnp.dot(
        placed_in.astype(jnp.float32), products.reshape(slots, -1), precision=HIGH
    ).reshape((total_rows,) + products.shape[1:])
    spread = lax.all_to_all(whole, "tile", 0, 0, tiled=True)
    partials = spread.reshape((group, owned) + spread.shape[1:]).sum(axis=0)
    row_work = (row_rhs[0].astype(jnp.float32) - partials).astype(jnp.bfloat16)
    row_values = jnp.einsum(
        "irb,ibc->irc", row_work, row_inverse[0], preferred_element_type=jnp.float32
    )
    return (multipliers[None], bus_values[None], row_values[None])


def solution(mesh):
    placed = (
        P("tm", "tile"),
        P("tm", "tile"),
        P("tm", "tile"),
        P("tm", "tile", None, None),
        P("tm", "tile", None, None),
        P("tm", "tile", None, None),
        P("tm", "tile", None, None),
        P("tm", "tile", None, None),
        P("tm", "tile", None, None),
        P("tm", None, None),
        P("tm", None, None),
        P("tm", None, None),
    )
    return jax.shard_map(
        per_device,
        mesh=mesh,
        in_specs=placed,
        out_specs=(P("tm", None, None), P("tm", "tile", None, None), P("tm", "tile", None, None)),
        check_vma=False,
    )
```

```python
import jax
import jax.numpy as jnp
from jax import lax
from jax.sharding import PartitionSpec as P

HIGH = lax.Precision.HIGHEST
MID = lax.Precision.HIGH


def pulled_from(x, axis, by):
    size = lax.axis_size(axis)
    pairs = [(i + by, i) for i in range(size) if i + by < size]
    return lax.ppermute(x, axis, pairs)


def chain_multipliers(inverse, nextmat, rhside):
    vectors = rhside.shape[0]
    b = jnp.dot(rhside, inverse, precision=MID)
    a = -jnp.dot(nextmat, inverse, precision=MID)
    size = lax.axis_size("tm")
    by = 1
    if size >= 8:
        held = jnp.concatenate([b, a], axis=0)
        got = [pulled_from(held, "tm", k) for k in (1, 2, 3)]
        carry = got[2]
        for step in (got[1], got[0], held):
            carry = jnp.dot(carry, step[vectors:], precision=HIGH)
            carry = carry.at[:vectors].add(step[:vectors])
        b, a = carry[:vectors], carry[vectors:]
        by = 4
    while by < size:
        if by * 4 == size:
            b = b + jnp.dot(pulled_from(b, "tm", by), a, precision=HIGH)
            ahead = jnp.dot(pulled_from(b, "tm", by), a, precision=HIGH)
            b = b + jnp.dot(pulled_from(ahead, "tm", by), a, precision=HIGH)
            break
        got = pulled_from(jnp.concatenate([b, a], axis=0), "tm", by)
        got_b, got_a = got[:vectors], got[vectors:]
        b = b + jnp.dot(got_b, a, precision=HIGH)
        if by * 2 < size:
            a = jnp.dot(got_a, a, precision=HIGH)
        by *= 2
    return b


def per_device(
    tile_rows,
    tile_cols,
    live_tiles,
    factor_tiles,
    bus_inverse,
    bus_coupling,
    bus_rhs,
    row_inverse,
    row_rhs,
    coupling_inverse,
    coupling_next,
    coupling_rhs,
):
    multipliers = chain_multipliers(coupling_inverse[0], coupling_next[0], coupling_rhs[0])
    rounded = multipliers.astype(jnp.bfloat16)
    coupled = jnp.einsum(
        "rb,jbc->jrc", rounded, bus_coupling[0], preferred_element_type=jnp.float32
    )
    bus_work = (bus_rhs[0].astype(jnp.float32) - coupled).astype(jnp.bfloat16)
    bus_values = jnp.einsum(
        "jrb,jbc->jrc", bus_work, bus_inverse[0], preferred_element_type=jnp.float32
    ).astype(jnp.bfloat16)
    rows = tile_rows[0]
    cols = tile_cols[0]
    slots = rows.shape[0]
    chosen = jnp.take(bus_values, cols, axis=0)
    live = jnp.arange(slots) < live_tiles[0, 0]
    products = jnp.einsum(
        "krb,kbc->krc", chosen, factor_tiles[0], preferred_element_type=jnp.float32
    )
    owned = row_rhs.shape[1]
    group = lax.axis_size("tile")
    total_rows = owned * group
    placed_in = (jnp.arange(total_rows)[:, None] == rows[None, :]) & live[None, :]
    whole = jnp.dot(
        placed_in.astype(jnp.float32), products.reshape(slots, -1), precision=MID
    ).reshape((total_rows,) + products.shape[1:])
    spread = lax.all_to_all(whole, "tile", 0, 0, tiled=True)
    partials = spread.reshape((group, owned) + spread.shape[1:]).sum(axis=0)
    row_work = (row_rhs[0].astype(jnp.float32) - partials).astype(jnp.bfloat16)
    row_values = jnp.einsum(
        "irb,ibc->irc", row_work, row_inverse[0], preferred_element_type=jnp.float32
    )
    return (multipliers[None], bus_values[None], row_values[None])


def solution(mesh):
    placed = (
        P("tm", "tile"),
        P("tm", "tile"),
        P("tm", "tile"),
        P("tm", "tile", None, None),
        P("tm", "tile", None, None),
        P("tm", "tile", None, None),
        P("tm", "tile", None, None),
        P("tm", "tile", None, None),
        P("tm", "tile", None, None),
        P("tm", None, None),
        P("tm", None, None),
        P("tm", None, None),
    )
    return jax.shard_map(
        per_device,
        mesh=mesh,
        in_specs=placed,
        out_specs=(P("tm", None, None), P("tm", "tile", None, None), P("tm", "tile", None, None)),
        check_vma=False,
    )
```

```python
import jax
import jax.numpy as jnp
from jax import lax
from jax.sharding import PartitionSpec as P

HIGH = lax.Precision.HIGHEST
MID = lax.Precision.HIGH


def pulled_from(x, axis, by):
    size = lax.axis_size(axis)
    pairs = [(i + by, i) for i in range(size) if i + by < size]
    return lax.ppermute(x, axis, pairs)


def chain_multipliers(inverse, nextmat, rhside):
    vectors = rhside.shape[0]
    b = jnp.dot(rhside, inverse, precision=HIGH)
    a = -jnp.dot(nextmat, inverse, precision=HIGH)
    size = lax.axis_size("tm")
    by = 1
    if size >= 8:
        held = jnp.concatenate([b, a], axis=0)
        got = [pulled_from(held, "tm", k) for k in (1, 2, 3)]
        carry = got[2]
        for step in (got[1], got[0], held):
            carry = jnp.dot(carry, step[vectors:], precision=HIGH)
            carry = carry.at[:vectors].add(step[:vectors])
        b, a = carry[:vectors], carry[vectors:]
        by = 4
    while by < size:
        if by * 4 == size:
            b = b + jnp.dot(pulled_from(b, "tm", by), a, precision=HIGH)
            ahead = jnp.dot(pulled_from(b, "tm", by), a, precision=HIGH)
            b = b + jnp.dot(pulled_from(ahead, "tm", by), a, precision=HIGH)
            break
        got = pulled_from(jnp.concatenate([b, a], axis=0), "tm", by)
        got_b, got_a = got[:vectors], got[vectors:]
        b = b + jnp.dot(got_b, a, precision=HIGH)
        if by * 2 < size:
            a = jnp.dot(got_a, a, precision=HIGH)
        by *= 2
    return b


def per_device(
    tile_rows,
    tile_cols,
    live_tiles,
    factor_tiles,
    bus_inverse,
    bus_coupling,
    bus_rhs,
    row_inverse,
    row_rhs,
    coupling_inverse,
    coupling_next,
    coupling_rhs,
):
    multipliers = chain_multipliers(coupling_inverse[0], coupling_next[0], coupling_rhs[0])
    rounded = multipliers.astype(jnp.bfloat16)
    coupled = jnp.einsum(
        "rb,jbc->jrc", rounded, bus_coupling[0], preferred_element_type=jnp.float32
    )
    bus_work = (bus_rhs[0].astype(jnp.float32) - coupled).astype(jnp.bfloat16)
    bus_values = jnp.einsum(
        "jrb,jbc->jrc", bus_work, bus_inverse[0], preferred_element_type=jnp.float32
    ).astype(jnp.bfloat16)
    rows = tile_rows[0]
    cols = tile_cols[0]
    slots = rows.shape[0]
    chosen = jnp.take(bus_values, cols, axis=0)
    live = jnp.arange(slots) < live_tiles[0, 0]
    products = jnp.einsum(
        "krb,kbc->krc", chosen, factor_tiles[0], preferred_element_type=jnp.float32
    )
    owned = row_rhs.shape[1]
    group = lax.axis_size("tile")
    total_rows = owned * group
    placed_in = (jnp.arange(total_rows)[:, None] == rows[None, :]) & live[None, :]
    whole = jnp.dot(
        placed_in.astype(jnp.float32), products.reshape(slots, -1), precision=MID
    ).reshape((total_rows,) + products.shape[1:])
    spread = lax.all_to_all(whole, "tile", 0, 0, tiled=True)
    partials = spread.reshape((group, owned) + spread.shape[1:]).sum(axis=0)
    row_work = (row_rhs[0].astype(jnp.float32) - partials).astype(jnp.bfloat16)
    row_values = jnp.einsum(
        "irb,ibc->irc", row_work, row_inverse[0], preferred_element_type=jnp.float32
    )
    return (multipliers[None], bus_values[None], row_values[None])


def solution(mesh):
    placed = (
        P("tm", "tile"),
        P("tm", "tile"),
        P("tm", "tile"),
        P("tm", "tile", None, None),
        P("tm", "tile", None, None),
        P("tm", "tile", None, None),
        P("tm", "tile", None, None),
        P("tm", "tile", None, None),
        P("tm", "tile", None, None),
        P("tm", None, None),
        P("tm", None, None),
        P("tm", None, None),
    )
    return jax.shard_map(
        per_device,
        mesh=mesh,
        in_specs=placed,
        out_specs=(P("tm", None, None), P("tm", "tile", None, None), P("tm", "tile", None, None)),
        check_vma=False,
    )
```
